128 devices in a mesh: dp: 4 (over z), expert: 32 (over x, y, core).
Axes of the slice: x: 4, y: 4, z: 4, core: 2. Of those that a mesh axis runs over, the one named last changes fastest.
Arguments:
- tokens: bfloat16 [8192, 4096], P('expert', 'dp'), may hold values from -6 to 6
- targets: bfloat16 [8192, 4096], P('expert', 'dp'), may hold values from -4 to 4
- expert_ids: int32 [8192, 2], P('expert'), may hold values from 0 to 31, all different within a row; in each aligned block of 256 rows (0 to 255, 256 to 511, ...) at most 32 rows name the same one
- gate_weights: float32 [8192, 2], P('expert'), may hold values from 0.2 to 1
- level_weights: float32 [8192], P('expert'), may hold values from 0.2 to 2
- w_gate: bfloat16 [32, 4096, 1024], P('expert', 'dp'), may hold values from -0.09375 to 0.09375
- w_up: bfloat16 [32, 4096, 1024], P('expert', 'dp'), may hold values from -0.09375 to 0.09375
- w_down: bfloat16 [32, 1024, 4096], P('expert', None, 'dp'), may hold values from -0.1875 to 0.1875
Outputs:
- mixed: bfloat16 [8192, 4096], P('expert', 'dp')
- token_grad: bfloat16 [8192, 4096], P('expert', 'dp')
- gate_grads: float32 [32, 4096, 1024], P('expert', 'dp')
- up_grads: float32 [32, 4096, 1024], P('expert', 'dp')
- down_grads: float32 [32, 1024, 4096], P('expert', None, 'dp')
The draws below stay inside these ranges and needn't reach their ends.
Inputs may be any that keep to these rules, and one draw needn't show every extreme that they name: `expert_ids`: each row names two different experts. Among the rows of one device no expert is named more than 32 times, a bound that some block reaches.
All inputs are finite; a program needn't handle non-finite values.
Results may differ from the reference program's by a relative error of at most 0.0065.
Values may be sent and summed in bfloat16 or wider, within the bound.
No kernel may reach another device: no remote copies, remote signals or barrier semaphores. Data moves between devices by JAX's collectives and lax.ppermute only.
A program may use at most 128 MiB of HBM per device.

```python
import math
import jax
import jax.numpy as jnp
import numpy as np
from jax import lax

D = 4096
FF = 1024
TOK_DEV = 256
EXPERTS = 32
CAP = 32
SLOTS = 1024
TOKENS = 8192
N_EXPERT = 32


def level_of(key, extent, split, smallest, high):
    def one(position, shards_of):
        draws = jax.random.uniform(jax.random.fold_in(jax.random.fold_in(key, 6), position), (shards_of,), jnp.float32, smallest / len(split), high / len(split))
        return jnp.repeat(jnp.exp(draws), extent[position] // shards_of).reshape((-1,) + (1,) * (len(extent) - position - 1))

    factor_of = one(*split[0])
    for cut in split[1:]:
        factor_of = factor_of * one(*cut)
    return factor_of


def routed_block(stream_key, own, number, rows, count, top, limit, slope):
    order = jax.random.permutation(stream_key, count)
    crowded, usual = load_shares(count, rows * top, limit, slope, True), load_shares(count, rows * top, limit, slope, False)
    places = jnp.arange(count)

    def named(lengths, turn):
        used = int((lengths > 0).sum())
        fixed = max(1, used // 4)
        shifted = fixed + (places - fixed + turn * (used - fixed)) % max(1, count - fixed)
        return jnp.zeros((count,), jnp.int32).at[order[jnp.where(places < fixed, places, shifted)]].set(jnp.asarray(lengths, jnp.int32))

    lengths = jnp.where(number % 4 == 0, named(crowded, number // 4), named(usual, number - number // 4 - 1))
    mixed = jax.random.permutation(jax.random.fold_in(own, 3), count)
    source_of, receiver = mixed[0:count // 2 * 2:2], mixed[1:count // 2 * 2:2]
    slack = jnp.minimum(lengths[source_of] - 1, limit - lengths[receiver]) // 2
    slack = jnp.where((source_of == order[0]) | (receiver == order[0]) | (lengths[receiver] == 0), 0, jnp.maximum(slack, 0))
    shifted = jax.random.randint(jax.random.fold_in(own, 4), (count // 2,), 0, 1 << 20) % (slack + 1)
    lengths = lengths.at[source_of].add(-shifted).at[receiver].add(shifted)
    members = jnp.searchsorted(jnp.cumsum(lengths), jnp.arange(rows * top), side="right").astype(jnp.int32)
    table = members.reshape(top, rows).T
    table = table[jax.random.permutation(jax.random.fold_in(own, 1), rows)]
    turn = jax.random.randint(jax.random.fold_in(own, 2), (rows, 1), 0, top)
    return jnp.take_along_axis(table, (jnp.arange(top)[None, :] + turn) % top, axis=1)


def load_shares(number_of, total, reach, slope, full):
    weights = [(1 << 20) // math.isqrt(standing ** slope) + 1 for standing in range(1, number_of + 1)]
    largest = reach if full else min(reach, max(-(-total // number_of), total * weights[0] // sum(weights)))
    least = 1 if total - largest >= number_of - 1 else 0
    counts, surplus = [largest] + [least] * (number_of - 1), total - largest - least * (number_of - 1)
    while surplus > 0:
        free = [i for i in range(1, number_of) if counts[i] < largest] or [i for i in range(1, number_of) if counts[i] < reach]
        mass, remaining = sum([weights[i] for i in free]), surplus
        for i in free:
            addition = min(reach - counts[i], max(1, remaining * weights[i] // mass), surplus)
            counts[i] = counts[i] + addition
            surplus = surplus - addition
    return np.array(counts)


def normal_values(own_key, dims, scale, most, cuts=(), kind=jnp.bfloat16):
    drawn = scale * jax.random.normal(own_key, dims, jnp.float32)
    if cuts:
        drawn = drawn * level_of(own_key, dims, cuts, -0.22, 0.18)
    return jnp.clip(drawn, -most, most).astype(kind)


def setup_inputs(seed: int = 0) -> dict:
    key_of = jax.random.split(jax.random.key(seed), 9)
    tokens = normal_values(key_of[0], (TOKENS, D), 1.0, 6.0, ((0, 32), (1, 4)))
    targets = normal_values(key_of[1], (TOKENS, D), 0.5, 4.0, ((0, 32), (1, 4)))
    expert_ids_keys = jax.random.split(jax.random.fold_in(key_of[2], 1), TOKENS // TOK_DEV)
    expert_ids_turns = jax.random.permutation(jax.random.fold_in(key_of[2], 3), TOKENS // TOK_DEV)
    expert_ids = jax.vmap(lambda own, number: routed_block(jax.random.fold_in(key_of[2], 2), own, number, TOK_DEV, EXPERTS, 2, CAP, 2))(expert_ids_keys, expert_ids_turns).reshape((TOKENS, 2))
    gate_weights = jnp.clip(0.2 + 0.8 * jax.random.uniform(key_of[3], (TOKENS, 2), jnp.float32) ** level_of(key_of[3], (TOKENS, 2), ((0, 32),), -0.2, 0.2), 0.2, 1.0)
    level_weights = jnp.clip(jnp.exp(math.log(2.0) - 2.3025851 * jax.random.uniform(key_of[4], (TOKENS,), jnp.float32) ** level_of(key_of[4], (TOKENS,), ((0, 32),), -0.2, 0.2)), 0.2, 2.0)
    w_gate = normal_values(key_of[5], (EXPERTS, D, FF), D ** -0.5, 0.09375, ((0, 32), (1, 4)))
    w_up = normal_values(key_of[6], (EXPERTS, D, FF), D ** -0.5, 0.09375, ((0, 32), (1, 4)))
    w_down = normal_values(key_of[7], (EXPERTS, FF, D), FF ** -0.5, 0.1875, ((0, 32), (2, 4)))
    return {"tokens": tokens, "targets": targets, "expert_ids": expert_ids, "gate_weights": gate_weights, "level_weights": level_weights, "w_gate": w_gate, "w_up": w_up, "w_down": w_down}


def slot_ranks(routing, experts):
    listed = routing.reshape(routing.shape[0], -1)
    onehot = (listed[:, :, None] == jnp.arange(experts, dtype=jnp.int32)[None, None, :]).astype(jnp.int32)
    earlier = jnp.cumsum(onehot, axis=1) - onehot
    return jnp.sum(earlier * onehot, axis=2).astype(jnp.int32)


def reference(tokens, targets, expert_ids, gate_weights, level_weights, w_gate, w_up, w_down):
    routing = expert_ids.reshape(N_EXPERT, TOK_DEV, 2)
    ranks = slot_ranks(routing, EXPERTS).reshape(-1)
    listed = expert_ids.reshape(-1).astype(jnp.int32)
    blocks = (jnp.arange(2 * TOKENS, dtype=jnp.int32) // (2 * TOK_DEV)).astype(jnp.int32)
    places = (blocks * CAP + ranks).astype(jnp.int32)
    spread = jnp.repeat(tokens, 2, axis=0)

    def scatter_rows(values, which):
        chosen = jnp.where(listed == which, places, SLOTS)
        return jnp.zeros((SLOTS, D), jnp.bfloat16).at[chosen].set(values, mode="drop")

    def projections(which):
        inputs = scatter_rows(spread, which)
        gate_pre = jnp.dot(inputs, w_gate[which], preferred_element_type=jnp.float32)
        up_pre = jnp.dot(inputs, w_up[which], preferred_element_type=jnp.float32)
        sigmoid_gate = jax.nn.sigmoid(gate_pre)
        hidden = (gate_pre * sigmoid_gate * up_pre).astype(jnp.bfloat16)
        return inputs, gate_pre, up_pre, sigmoid_gate, hidden

    def forward(which):
        hidden = projections(which)[4]
        return jnp.dot(hidden, w_down[which], preferred_element_type=jnp.float32).astype(jnp.bfloat16)

    everyone = jnp.arange(EXPERTS, dtype=jnp.int32)
    outputs = lax.map(forward, everyone)
    picked = outputs[listed, places].reshape(TOKENS, 2, D).astype(jnp.float32)
    combined = jnp.sum(gate_weights[:, :, None] * picked, axis=1)
    mixed = combined.astype(jnp.bfloat16)
    row_grad = level_weights[:, None] * (combined - targets.astype(jnp.float32))
    slot_grad = (gate_weights[:, :, None] * row_grad[:, None, :]).astype(jnp.bfloat16).reshape(2 * TOKENS, D)

    def backward(which):
        inputs, gate_pre, up_pre, sigmoid_gate, hidden = projections(which)
        arrived = scatter_rows(slot_grad, which)
        hidden_grad = jnp.dot(arrived, w_down[which].T, preferred_element_type=jnp.float32)
        gate_delta = (hidden_grad * up_pre * sigmoid_gate * (1.0 + gate_pre * (1.0 - sigmoid_gate))).astype(jnp.bfloat16)
        up_delta = (hidden_grad * gate_pre * sigmoid_gate).astype(jnp.bfloat16)
        input_grad = (jnp.dot(gate_delta, w_gate[which].T, preferred_element_type=jnp.float32)
                      + jnp.dot(up_delta, w_up[which].T, preferred_element_type=jnp.float32)).astype(jnp.bfloat16)
        gate_grad = jnp.dot(inputs.T, gate_delta, preferred_element_type=jnp.float32)
        up_grad = jnp.dot(inputs.T, up_delta, preferred_element_type=jnp.float32)
        down_grad = jnp.dot(hidden.T, arrived, preferred_element_type=jnp.float32)
        return input_grad, gate_grad, up_grad, down_grad

    input_grads, gate_grads, up_grads, down_grads = lax.map(backward, everyone)
    picked_grads = input_grads[listed, places].reshape(TOKENS, 2, D).astype(jnp.float32)
    token_grad = jnp.sum(picked_grads, axis=1).astype(jnp.bfloat16)
    return (mixed, token_grad, gate_grads, up_grads, down_grads)
```

```python
import jax
import jax.numpy as jnp
from jax import lax
from jax.sharding import PartitionSpec as P


def slot_ranks(routing, experts):
    listed = routing.reshape(routing.shape[0], -1)
    onehot = (listed[:, :, None] == jnp.arange(experts, dtype=jnp.int32)[None, None, :]).astype(
        jnp.int32
    )
    earlier = jnp.cumsum(onehot, axis=1) - onehot
    return jnp.sum(earlier * onehot, axis=2)


def contract(left, right, left_dim, right_dim):
    return lax.dot_general(
        left, right, (((left_dim,), (right_dim,)), ((), ())), preferred_element_type=jnp.float32
    )


def activate(gate_pre, up_pre):
    sigmoid_gate = jax.nn.sigmoid(gate_pre)
    return (sigmoid_gate, (gate_pre * sigmoid_gate * up_pre).astype(jnp.bfloat16))


def derivatives(hidden_grad, gate_pre, up_pre, sigmoid_gate):
    gate_delta = (
        hidden_grad * up_pre * sigmoid_gate * (1.0 + gate_pre * (1.0 - sigmoid_gate))
    ).astype(jnp.bfloat16)
    up_delta = (hidden_grad * gate_pre * sigmoid_gate).astype(jnp.bfloat16)
    return (gate_delta, up_delta)


def shards(tokens, targets, expert_ids, gate_weights, level_weights, w_gate, w_up, w_down):
    experts = lax.axis_size("expert")
    tok_rows = tokens.shape[0]
    quarter = tokens.shape[1]
    capacity = 4 * tok_rows // experts
    rows_all = experts * capacity
    gate_mat = w_gate[0]
    up_mat = w_up[0]
    down_mat = w_down[0]
    ranks = slot_ranks(expert_ids.reshape(1, tok_rows, 2), experts).reshape(-1)
    slot_rows = expert_ids.reshape(-1) * capacity + ranks
    spread = jnp.repeat(tokens, 2, axis=0)
    outgoing = jnp.zeros((rows_all, quarter), jnp.bfloat16).at[slot_rows].set(spread)
    arrived = lax.all_to_all(
        outgoing.reshape(experts, capacity, quarter),
        "expert",
        split_axis=0,
        concat_axis=0,
        tiled=True,
    ).reshape(rows_all, quarter)
    gate_pre, up_pre = lax.psum_scatter(
        (contract(arrived, gate_mat, 1, 0), contract(arrived, up_mat, 1, 0)),
        "dp",
        scatter_dimension=0,
        tiled=True,
    )
    sigmoid_gate, hidden_part = activate(gate_pre, up_pre)
    hidden = lax.all_gather(hidden_part, "dp", axis=0, tiled=True)
    out_slots = (
        contract(hidden, down_mat, 1, 0).astype(jnp.bfloat16).reshape(experts, capacity, quarter)
    )
    returned = lax.all_to_all(out_slots, "expert", split_axis=0, concat_axis=0, tiled=True).reshape(
        rows_all, quarter
    )
    picked = returned[slot_rows].reshape(tok_rows, 2, quarter).astype(jnp.float32)
    combined = jnp.sum(gate_weights[:, :, None] * picked, axis=1)
    mixed = combined.astype(jnp.bfloat16)
    row_grad = level_weights[:, None] * (combined - targets.astype(jnp.float32))
    slot_grad = (
        (gate_weights[:, :, None] * row_grad[:, None, :])
        .astype(jnp.bfloat16)
        .reshape(2 * tok_rows, quarter)
    )
    grad_out = jnp.zeros((rows_all, quarter), jnp.bfloat16).at[slot_rows].set(slot_grad)
    grad_slots = lax.all_to_all(
        grad_out.reshape(experts, capacity, quarter),
        "expert",
        split_axis=0,
        concat_axis=0,
        tiled=True,
    ).reshape(rows_all, quarter)
    down_grad = contract(hidden, grad_slots, 0, 0)
    hidden_grad = lax.psum_scatter(
        contract(grad_slots, down_mat, 1, 1), "dp", scatter_dimension=0, tiled=True
    )
    gate_part, up_part = derivatives(hidden_grad, gate_pre, up_pre, sigmoid_gate)
    gate_delta, up_delta = lax.all_gather((gate_part, up_part), "dp", axis=0, tiled=True)
    input_slots = (contract(gate_delta, gate_mat, 1, 1) + contract(up_delta, up_mat, 1, 1)).astype(
        jnp.bfloat16
    )
    gate_grad = contract(arrived, gate_delta, 0, 0)
    up_grad = contract(arrived, up_delta, 0, 0)
    input_back = lax.all_to_all(
        input_slots.reshape(experts, capacity, quarter),
        "expert",
        split_axis=0,
        concat_axis=0,
        tiled=True,
    ).reshape(rows_all, quarter)
    token_grad = jnp.sum(
        input_back[slot_rows].reshape(tok_rows, 2, quarter).astype(jnp.float32), axis=1
    ).astype(jnp.bfloat16)
    return (mixed, token_grad, gate_grad[None], up_grad[None], down_grad[None])


def solution(mesh):
    in_specs = (
        P("expert", "dp"),
        P("expert", "dp"),
        P("expert", None),
        P("expert", None),
        P("expert"),
        P("expert", "dp", None),
        P("expert", "dp", None),
        P("expert", None, "dp"),
    )
    out_specs = (
        P("expert", "dp"),
        P("expert", "dp"),
        P("expert", "dp", None),
        P("expert", "dp", None),
        P("expert", None, "dp"),
    )
    return jax.shard_map(shards, mesh=mesh, in_specs=in_specs, out_specs=out_specs, check_vma=False)
```

```python
import jax
import jax.numpy as jnp
from jax import lax
from jax.sharding import PartitionSpec as P


def slot_ranks(routing, experts):
    listed = routing.reshape(routing.shape[0], -1)
    onehot = (listed[:, :, None] == jnp.arange(experts, dtype=jnp.int32)[None, None, :]).astype(
        jnp.int32
    )
    earlier = jnp.cumsum(onehot, axis=1) - onehot
    return jnp.sum(earlier * onehot, axis=2)


def contract(left, right, left_dim, right_dim):
    return lax.dot_general(
        left, right, (((left_dim,), (right_dim,)), ((), ())), preferred_element_type=jnp.float32
    )


def activate(gate_pre, up_pre):
    sigmoid_gate = jax.nn.sigmoid(gate_pre)
    return (sigmoid_gate, (gate_pre * sigmoid_gate * up_pre).astype(jnp.bfloat16))


def derivatives(hidden_grad, gate_pre, up_pre, sigmoid_gate):
    gate_delta = (
        hidden_grad * up_pre * sigmoid_gate * (1.0 + gate_pre * (1.0 - sigmoid_gate))
    ).astype(jnp.bfloat16)
    up_delta = (hidden_grad * gate_pre * sigmoid_gate).astype(jnp.bfloat16)
    return (gate_delta, up_delta)


def dp_reduce_scatter(parts):
    peers = lax.axis_size("dp")
    pieces = parts.astype(jnp.bfloat16).reshape(peers, parts.shape[0] // peers, parts.shape[1])
    got = lax.all_to_all(pieces, "dp", split_axis=0, concat_axis=0, tiled=True)
    return jnp.sum(got.astype(jnp.float32), axis=0)


def shards(tokens, targets, expert_ids, gate_weights, level_weights, w_gate, w_up, w_down):
    experts = lax.axis_size("expert")
    tok_rows = tokens.shape[0]
    quarter = tokens.shape[1]
    capacity = 4 * tok_rows // experts
    rows_all = experts * capacity
    gate_mat = w_gate[0]
    up_mat = w_up[0]
    down_mat = w_down[0]
    ranks = slot_ranks(expert_ids.reshape(1, tok_rows, 2), experts).reshape(-1)
    slot_rows = expert_ids.reshape(-1) * capacity + ranks
    spread = jnp.repeat(tokens, 2, axis=0)
    outgoing = jnp.zeros((rows_all, quarter), jnp.bfloat16).at[slot_rows].set(spread)
    arrived = lax.all_to_all(
        outgoing.reshape(experts, capacity, quarter),
        "expert",
        split_axis=0,
        concat_axis=0,
        tiled=True,
    ).reshape(rows_all, quarter)
    ff = gate_mat.shape[1]
    both = dp_reduce_scatter(
        jnp.concatenate([contract(arrived, gate_mat, 1, 0), contract(arrived, up_mat, 1, 0)], axis=1)
    )
    gate_pre, up_pre = both[:, :ff], both[:, ff:]
    sigmoid_gate, hidden_part = activate(gate_pre, up_pre)
    hidden = lax.all_gather(hidden_part, "dp", axis=0, tiled=True)
    out_slots = (
        contract(hidden, down_mat, 1, 0).astype(jnp.bfloat16).reshape(experts, capacity, quarter)
    )
    returned = lax.all_to_all(out_slots, "expert", split_axis=0, concat_axis=0, tiled=True).reshape(
        rows_all, quarter
    )
    picked = returned[slot_rows].reshape(tok_rows, 2, quarter).astype(jnp.float32)
    combined = jnp.sum(gate_weights[:, :, None] * picked, axis=1)
    mixed = combined.astype(jnp.bfloat16)
    row_grad = level_weights[:, None] * (combined - targets.astype(jnp.float32))
    slot_grad = (
        (gate_weights[:, :, None] * row_grad[:, None, :])
        .astype(jnp.bfloat16)
        .reshape(2 * tok_rows, quarter)
    )
    grad_out = jnp.zeros((rows_all, quarter), jnp.bfloat16).at[slot_rows].set(slot_grad)
    grad_slots = lax.all_to_all(
        grad_out.reshape(experts, capacity, quarter),
        "expert",
        split_axis=0,
        concat_axis=0,
        tiled=True,
    ).reshape(rows_all, quarter)
    down_grad = contract(hidden, grad_slots, 0, 0)
    hidden_grad = dp_reduce_scatter(contract(grad_slots, down_mat, 1, 1))
    gate_part, up_part = derivatives(hidden_grad, gate_pre, up_pre, sigmoid_gate)
    gate_delta, up_delta = lax.all_gather((gate_part, up_part), "dp", axis=0, tiled=True)
    input_slots = (contract(gate_delta, gate_mat, 1, 1) + contract(up_delta, up_mat, 1, 1)).astype(
        jnp.bfloat16
    )
    gate_grad = contract(arrived, gate_delta, 0, 0)
    up_grad = contract(arrived, up_delta, 0, 0)
    input_back = lax.all_to_all(
        input_slots.reshape(experts, capacity, quarter),
        "expert",
        split_axis=0,
        concat_axis=0,
        tiled=True,
    ).reshape(rows_all, quarter)
    token_grad = jnp.sum(
        input_back[slot_rows].reshape(tok_rows, 2, quarter).astype(jnp.float32), axis=1
    ).astype(jnp.bfloat16)
    return (mixed, token_grad, gate_grad[None], up_grad[None], down_grad[None])


def solution(mesh):
    in_specs = (
        P("expert", "dp"),
        P("expert", "dp"),
        P("expert", None),
        P("expert", None),
        P("expert"),
        P("expert", "dp", None),
        P("expert", "dp", None),
        P("expert", None, "dp"),
    )
    out_specs = (
        P("expert", "dp"),
        P("expert", "dp"),
        P("expert", "dp", None),
        P("expert", "dp", None),
        P("expert", None, "dp"),
    )
    return jax.shard_map(shards, mesh=mesh, in_specs=in_specs, out_specs=out_specs, check_vma=False)
```

```python
import jax
import jax.numpy as jnp
from jax import lax
from jax.sharding import PartitionSpec as P


def slot_ranks(routing, experts):
    listed = routing.reshape(routing.shape[0], -1)
    onehot = (listed[:, :, None] == jnp.arange(experts, dtype=jnp.int32)[None, None, :]).astype(
        jnp.int32
    )
    earlier = jnp.cumsum(onehot, axis=1) - onehot
    return jnp.sum(earlier * onehot, axis=2)


def contract(left, right, left_dim, right_dim):
    return lax.dot_general(
        left, right, (((left_dim,), (right_dim,)), ((), ())), preferred_element_type=jnp.float32
    )


def activate(gate_pre, up_pre):
    sigmoid_gate = jax.nn.sigmoid(gate_pre)
    return (sigmoid_gate, (gate_pre * sigmoid_gate * up_pre).astype(jnp.bfloat16))


def derivatives(hidden_grad, gate_pre, up_pre, sigmoid_gate):
    gate_delta = (
        hidden_grad * up_pre * sigmoid_gate * (1.0 + gate_pre * (1.0 - sigmoid_gate))
    ).astype(jnp.bfloat16)
    up_delta = (hidden_grad * gate_pre * sigmoid_gate).astype(jnp.bfloat16)
    return (gate_delta, up_delta)


def expert_exchange(blocks):
    return lax.all_to_all(blocks, "expert", split_axis=0, concat_axis=0, tiled=True)


CHUNKS = 2


def shards(tokens, targets, expert_ids, gate_weights, level_weights, w_gate, w_up, w_down):
    experts = lax.axis_size("expert")
    tok_rows = tokens.shape[0]
    quarter = tokens.shape[1]
    capacity = 4 * tok_rows // experts
    rows_all = experts * capacity
    step = capacity // CHUNKS
    gate_mat = w_gate[0]
    up_mat = w_up[0]
    down_mat = w_down[0]
    ff = gate_mat.shape[1]
    ranks = slot_ranks(expert_ids.reshape(1, tok_rows, 2), experts).reshape(-1)
    slot_rows = expert_ids.reshape(-1) * capacity + ranks
    spread = jnp.repeat(tokens, 2, axis=0)
    outgoing = (
        jnp.zeros((rows_all, quarter), jnp.bfloat16)
        .at[slot_rows]
        .set(spread)
        .reshape(experts, capacity, quarter)
    )
    arrived, kept, returned = [], [], []
    for c in range(CHUNKS):
        got = expert_exchange(outgoing[:, c * step : (c + 1) * step]).reshape(-1, quarter)
        arrived.append(got)
        both = lax.psum_scatter(
            jnp.concatenate([contract(got, gate_mat, 1, 0), contract(got, up_mat, 1, 0)], axis=1),
            "dp",
            scatter_dimension=0,
            tiled=True,
        )
        gate_pre, up_pre = both[:, :ff], both[:, ff:]
        sigmoid_gate, hidden_part = activate(gate_pre, up_pre)
        hidden = lax.all_gather(hidden_part, "dp", axis=0, tiled=True)
        kept.append((gate_pre, up_pre, sigmoid_gate, hidden))
        out_slots = contract(hidden, down_mat, 1, 0).astype(jnp.bfloat16)
        returned.append(expert_exchange(out_slots.reshape(experts, step, quarter)))
    returned = jnp.concatenate(returned, axis=1).reshape(rows_all, quarter)
    picked = returned[slot_rows].reshape(tok_rows, 2, quarter).astype(jnp.float32)
    combined = jnp.sum(gate_weights[:, :, None] * picked, axis=1)
    mixed = combined.astype(jnp.bfloat16)
    row_grad = level_weights[:, None] * (combined - targets.astype(jnp.float32))
    slot_grad = (
        (gate_weights[:, :, None] * row_grad[:, None, :])
        .astype(jnp.bfloat16)
        .reshape(2 * tok_rows, quarter)
    )
    grad_out = (
        jnp.zeros((rows_all, quarter), jnp.bfloat16)
        .at[slot_rows]
        .set(slot_grad)
        .reshape(experts, capacity, quarter)
    )
    down_grad = gate_grad = up_grad = None
    input_back = []
    for c in range(CHUNKS):
        gate_pre, up_pre, sigmoid_gate, hidden = kept[c]
        grad_slots = expert_exchange(grad_out[:, c * step : (c + 1) * step]).reshape(-1, quarter)
        hidden_grad = lax.psum_scatter(
            contract(grad_slots, down_mat, 1, 1), "dp", scatter_dimension=0, tiled=True
        )
        deltas = lax.all_gather(
            jnp.concatenate(derivatives(hidden_grad, gate_pre, up_pre, sigmoid_gate), axis=1),
            "dp",
            axis=0,
            tiled=True,
        )
        gate_delta, up_delta = deltas[:, :ff], deltas[:, ff:]
        input_slots = (
            contract(gate_delta, gate_mat, 1, 1) + contract(up_delta, up_mat, 1, 1)
        ).astype(jnp.bfloat16)
        input_back.append(expert_exchange(input_slots.reshape(experts, step, quarter)))
        parts = (
            contract(hidden, grad_slots, 0, 0),
            contract(arrived[c], gate_delta, 0, 0),
            contract(arrived[c], up_delta, 0, 0),
        )
        if c == 0:
            down_grad, gate_grad, up_grad = parts
        else:
            down_grad, gate_grad, up_grad = (
                down_grad + parts[0],
                gate_grad + parts[1],
                up_grad + parts[2],
            )
    input_back = jnp.concatenate(input_back, axis=1).reshape(rows_all, quarter)
    token_grad = jnp.sum(
        input_back[slot_rows].reshape(tok_rows, 2, quarter).astype(jnp.float32), axis=1
    ).astype(jnp.bfloat16)
    return (mixed, token_grad, gate_grad[None], up_grad[None], down_grad[None])


def solution(mesh):
    in_specs = (
        P("expert", "dp"),
        P("expert", "dp"),
        P("expert", None),
        P("expert", None),
        P("expert"),
        P("expert", "dp", None),
        P("expert", "dp", None),
        P("expert", None, "dp"),
    )
    out_specs = (
        P("expert", "dp"),
        P("expert", "dp"),
        P("expert", "dp", None),
        P("expert", "dp", None),
        P("expert", None, "dp"),
    )
    return jax.shard_map(shards, mesh=mesh, in_specs=in_specs, out_specs=out_specs, check_vma=False)
```

```python
import jax
import jax.numpy as jnp
from jax import lax
from jax.sharding import PartitionSpec as P


def slot_ranks(routing, experts):
    listed = routing.reshape(routing.shape[0], -1)
    onehot = (listed[:, :, None] == jnp.arange(experts, dtype=jnp.int32)[None, None, :]).astype(
        jnp.int32
    )
    earlier = jnp.cumsum(onehot, axis=1) - onehot
    return jnp.sum(earlier * onehot, axis=2)


def contract(left, right, left_dim, right_dim):
    return lax.dot_general(
        left, right, (((left_dim,), (right_dim,)), ((), ())), preferred_element_type=jnp.float32
    )


def activate(gate_pre, up_pre):
    sigmoid_gate = jax.nn.sigmoid(gate_pre)
    return (sigmoid_gate, (gate_pre * sigmoid_gate * up_pre).astype(jnp.bfloat16))


def derivatives(hidden_grad, gate_pre, up_pre, sigmoid_gate):
    gate_delta = (
        hidden_grad * up_pre * sigmoid_gate * (1.0 + gate_pre * (1.0 - sigmoid_gate))
    ).astype(jnp.bfloat16)
    up_delta = (hidden_grad * gate_pre * sigmoid_gate).astype(jnp.bfloat16)
    return (gate_delta, up_delta)


def dp_reduce_scatter(parts):
    peers = lax.axis_size("dp")
    pieces = parts.astype(jnp.bfloat16).reshape(peers, parts.shape[0] // peers, parts.shape[1])
    got = lax.all_to_all(pieces, "dp", split_axis=0, concat_axis=0, tiled=True)
    return jnp.sum(got.astype(jnp.float32), axis=0)


def dp_all_gather(part):
    peers = lax.axis_size("dp")
    copies = jnp.broadcast_to(part[None], (peers,) + part.shape)
    got = lax.all_to_all(copies, "dp", split_axis=0, concat_axis=0, tiled=True)
    return got.reshape(peers * part.shape[0], part.shape[1])


def shards(tokens, targets, expert_ids, gate_weights, level_weights, w_gate, w_up, w_down):
    experts = lax.axis_size("expert")
    tok_rows = tokens.shape[0]
    quarter = tokens.shape[1]
    capacity = 4 * tok_rows // experts
    rows_all = experts * capacity
    gate_mat = w_gate[0]
    up_mat = w_up[0]
    down_mat = w_down[0]
    ranks = slot_ranks(expert_ids.reshape(1, tok_rows, 2), experts).reshape(-1)
    slot_rows = expert_ids.reshape(-1) * capacity + ranks
    spread = jnp.repeat(tokens, 2, axis=0)
    outgoing = jnp.zeros((rows_all, quarter), jnp.bfloat16).at[slot_rows].set(spread)
    arrived = lax.all_to_all(
        outgoing.reshape(experts, capacity, quarter),
        "expert",
        split_axis=0,
        concat_axis=0,
        tiled=True,
    ).reshape(rows_all, quarter)
    gate_pre = lax.psum_scatter(
        contract(arrived, gate_mat, 1, 0), "dp", scatter_dimension=0, tiled=True
    )
    up_pre = dp_reduce_scatter(contract(arrived, up_mat, 1, 0))
    sigmoid_gate, hidden_part = activate(gate_pre, up_pre)
    hidden = lax.all_gather(hidden_part, "dp", axis=0, tiled=True)
    out_slots = (
        contract(hidden, down_mat, 1, 0).astype(jnp.bfloat16).reshape(experts, capacity, quarter)
    )
    returned = lax.all_to_all(out_slots, "expert", split_axis=0, concat_axis=0, tiled=True).reshape(
        rows_all, quarter
    )
    picked = returned[slot_rows].reshape(tok_rows, 2, quarter).astype(jnp.float32)
    combined = jnp.sum(gate_weights[:, :, None] * picked, axis=1)
    mixed = combined.astype(jnp.bfloat16)
    row_grad = level_weights[:, None] * (combined - targets.astype(jnp.float32))
    slot_grad = (
        (gate_weights[:, :, None] * row_grad[:, None, :])
        .astype(jnp.bfloat16)
        .reshape(2 * tok_rows, quarter)
    )
    grad_out = jnp.zeros((rows_all, quarter), jnp.bfloat16).at[slot_rows].set(slot_grad)
    grad_slots = lax.all_to_all(
        grad_out.reshape(experts, capacity, quarter),
        "expert",
        split_axis=0,
        concat_axis=0,
        tiled=True,
    ).reshape(rows_all, quarter)
    down_grad = contract(hidden, grad_slots, 0, 0)
    half = down_mat.shape[0] // 2
    hidden_grad = jnp.concatenate(
        [
            lax.psum_scatter(
                contract(grad_slots, down_mat[:half], 1, 1), "dp", scatter_dimension=0, tiled=True
            ),
            dp_reduce_scatter(contract(grad_slots, down_mat[half:], 1, 1)),
        ],
        axis=1,
    )
    gate_part, up_part = derivatives(hidden_grad, gate_pre, up_pre, sigmoid_gate)
    gate_delta = lax.all_gather(gate_part, "dp", axis=0, tiled=True)
    up_delta = dp_all_gather(up_part)
    input_slots = (contract(gate_delta, gate_mat, 1, 1) + contract(up_delta, up_mat, 1, 1)).astype(
        jnp.bfloat16
    )
    gate_grad = contract(arrived, gate_delta, 0, 0)
    up_grad = contract(arrived, up_delta, 0, 0)
    input_back = lax.all_to_all(
        input_slots.reshape(experts, capacity, quarter),
        "expert",
        split_axis=0,
        concat_axis=0,
        tiled=True,
    ).reshape(rows_all, quarter)
    token_grad = jnp.sum(
        input_back[slot_rows].reshape(tok_rows, 2, quarter).astype(jnp.float32), axis=1
    ).astype(jnp.bfloat16)
    return (mixed, token_grad, gate_grad[None], up_grad[None], down_grad[None])


def solution(mesh):
    in_specs = (
        P("expert", "dp"),
        P("expert", "dp"),
        P("expert", None),
        P("expert", None),
        P("expert"),
        P("expert", "dp", None),
        P("expert", "dp", None),
        P("expert", None, "dp"),
    )
    out_specs = (
        P("expert", "dp"),
        P("expert", "dp"),
        P("expert", "dp", None),
        P("expert", "dp", None),
        P("expert", None, "dp"),
    )
    return jax.shard_map(shards, mesh=mesh, in_specs=in_specs, out_specs=out_specs, check_vma=False)
```

```python
import jax
import jax.numpy as jnp
from jax import lax
from jax.sharding import PartitionSpec as P


def slot_ranks(routing, experts):
    listed = routing.reshape(routing.shape[0], -1)
    onehot = (listed[:, :, None] == jnp.arange(experts, dtype=jnp.int32)[None, None, :]).astype(
        jnp.int32
    )
    earlier = jnp.cumsum(onehot, axis=1) - onehot
    return jnp.sum(earlier * onehot, axis=2)


def contract(left, right, left_dim, right_dim):
    return lax.dot_general(
        left, right, (((left_dim,), (right_dim,)), ((), ())), preferred_element_type=jnp.float32
    )


def activate(gate_pre, up_pre):
    sigmoid_gate = jax.nn.sigmoid(gate_pre)
    return (sigmoid_gate, (gate_pre * sigmoid_gate * up_pre).astype(jnp.bfloat16))


def derivatives(hidden_grad, gate_pre, up_pre, sigmoid_gate):
    gate_delta = (
        hidden_grad * up_pre * sigmoid_gate * (1.0 + gate_pre * (1.0 - sigmoid_gate))
    ).astype(jnp.bfloat16)
    up_delta = (hidden_grad * gate_pre * sigmoid_gate).astype(jnp.bfloat16)
    return (gate_delta, up_delta)


def shards(tokens, targets, expert_ids, gate_weights, level_weights, w_gate, w_up, w_down):
    experts = lax.axis_size("expert")
    tok_rows = tokens.shape[0]
    quarter = tokens.shape[1]
    capacity = 4 * tok_rows // experts
    rows_all = experts * capacity
    gate_mat = w_gate[0]
    up_mat = w_up[0]
    down_mat = w_down[0]
    ff = gate_mat.shape[1]
    ranks = slot_ranks(expert_ids.reshape(1, tok_rows, 2), experts).reshape(-1)
    slot_rows = expert_ids.reshape(-1) * capacity + ranks
    select = (slot_rows[:, None] == jnp.arange(rows_all, dtype=slot_rows.dtype)[None, :]).astype(
        jnp.bfloat16
    )
    per_token = jnp.sum(select.reshape(tok_rows, 2, rows_all), axis=1)
    outgoing = contract(per_token, tokens, 0, 0).astype(jnp.bfloat16)
    arrived = lax.all_to_all(
        outgoing.reshape(experts, capacity, quarter),
        "expert",
        split_axis=0,
        concat_axis=0,
        tiled=True,
    ).reshape(rows_all, quarter)
    both = lax.psum_scatter(
        jnp.concatenate([contract(arrived, gate_mat, 1, 0), contract(arrived, up_mat, 1, 0)], axis=1),
        "dp",
        scatter_dimension=0,
        tiled=True,
    )
    gate_pre, up_pre = both[:, :ff], both[:, ff:]
    sigmoid_gate, hidden_part = activate(gate_pre, up_pre)
    hidden = lax.all_gather(hidden_part, "dp", axis=0, tiled=True)
    out_slots = (
        contract(hidden, down_mat, 1, 0).astype(jnp.bfloat16).reshape(experts, capacity, quarter)
    )
    returned = lax.all_to_all(out_slots, "expert", split_axis=0, concat_axis=0, tiled=True).reshape(
        rows_all, quarter
    )
    picked = contract(select, returned, 1, 0).reshape(tok_rows, 2, quarter)
    combined = jnp.sum(gate_weights[:, :, None] * picked, axis=1)
    mixed = combined.astype(jnp.bfloat16)
    row_grad = level_weights[:, None] * (combined - targets.astype(jnp.float32))
    slot_grad = (
        (gate_weights[:, :, None] * row_grad[:, None, :])
        .astype(jnp.bfloat16)
        .reshape(2 * tok_rows, quarter)
    )
    grad_out = contract(select, slot_grad, 0, 0).astype(jnp.bfloat16)
    grad_slots = lax.all_to_all(
        grad_out.reshape(experts, capacity, quarter),
        "expert",
        split_axis=0,
        concat_axis=0,
        tiled=True,
    ).reshape(rows_all, quarter)
    down_grad = contract(hidden, grad_slots, 0, 0)
    hidden_grad = lax.psum_scatter(
        contract(grad_slots, down_mat, 1, 1), "dp", scatter_dimension=0, tiled=True
    )
    deltas = lax.all_gather(
        jnp.concatenate(derivatives(hidden_grad, gate_pre, up_pre, sigmoid_gate), axis=1),
        "dp",
        axis=0,
        tiled=True,
    )
    gate_delta, up_delta = deltas[:, :ff], deltas[:, ff:]
    input_slots = (contract(gate_delta, gate_mat, 1, 1) + contract(up_delta, up_mat, 1, 1)).astype(
        jnp.bfloat16
    )
    gate_grad = contract(arrived, gate_delta, 0, 0)
    up_grad = contract(arrived, up_delta, 0, 0)
    input_back = lax.all_to_all(
        input_slots.reshape(experts, capacity, quarter),
        "expert",
        split_axis=0,
        concat_axis=0,
        tiled=True,
    ).reshape(rows_all, quarter)
    token_grad = contract(per_token, input_back, 1, 0).astype(jnp.bfloat16)
    return (mixed, token_grad, gate_grad[None], up_grad[None], down_grad[None])


def solution(mesh):
    in_specs = (
        P("expert", "dp"),
        P("expert", "dp"),
        P("expert", None),
        P("expert", None),
        P("expert"),
        P("expert", "dp", None),
        P("expert", "dp", None),
        P("expert", None, "dp"),
    )
    out_specs = (
        P("expert", "dp"),
        P("expert", "dp"),
        P("expert", "dp", None),
        P("expert", "dp", None),
        P("expert", None, "dp"),
    )
    return jax.shard_map(shards, mesh=mesh, in_specs=in_specs, out_specs=out_specs, check_vma=False)
```

```python
import jax
import jax.numpy as jnp
from jax import lax
from jax.sharding import PartitionSpec as P


def slot_ranks(routing, experts):
    listed = routing.reshape(routing.shape[0], -1)
    onehot = (listed[:, :, None] == jnp.arange(experts, dtype=jnp.int32)[None, None, :]).astype(
        jnp.int32
    )
    earlier = jnp.cumsum(onehot, axis=1) - onehot
    return jnp.sum(earlier * onehot, axis=2)


def contract(left, right, left_dim, right_dim):
    return lax.dot_general(
        left, right, (((left_dim,), (right_dim,)), ((), ())), preferred_element_type=jnp.float32
    )


def activate(gate_pre, up_pre):
    sigmoid_gate = jax.nn.sigmoid(gate_pre)
    return (sigmoid_gate, (gate_pre * sigmoid_gate * up_pre).astype(jnp.bfloat16))


def derivatives(hidden_grad, gate_pre, up_pre, sigmoid_gate):
    gate_delta = (
        hidden_grad * up_pre * sigmoid_gate * (1.0 + gate_pre * (1.0 - sigmoid_gate))
    ).astype(jnp.bfloat16)
    up_delta = (hidden_grad * gate_pre * sigmoid_gate).astype(jnp.bfloat16)
    return (gate_delta, up_delta)


def ring_reduce_scatter(parts):
    peers = lax.axis_size("dp")
    me = lax.axis_index("dp")
    cols = parts.shape[1] // 2
    blocks = parts.reshape(peers, parts.shape[0] // peers, parts.shape[1])
    east, west = blocks[:, :, :cols], blocks[:, :, cols:]
    to_east = [(j, (j + 1) % peers) for j in range(peers)]
    to_west = [(j, (j - 1) % peers) for j in range(peers)]
    east_acc = east[(me - 1) % peers]
    west_acc = west[(me + 1) % peers]
    for s in range(peers - 1):
        east_acc = lax.ppermute(east_acc, "dp", to_east) + east[(me - s - 2) % peers]
        west_acc = lax.ppermute(west_acc, "dp", to_west) + west[(me + s + 2) % peers]
    return jnp.concatenate([east_acc, west_acc], axis=1)


def shards(tokens, targets, expert_ids, gate_weights, level_weights, w_gate, w_up, w_down):
    experts = lax.axis_size("expert")
    tok_rows = tokens.shape[0]
    quarter = tokens.shape[1]
    capacity = 4 * tok_rows // experts
    rows_all = experts * capacity
    gate_mat = w_gate[0]
    up_mat = w_up[0]
    down_mat = w_down[0]
    ff = gate_mat.shape[1]
    ranks = slot_ranks(expert_ids.reshape(1, tok_rows, 2), experts).reshape(-1)
    slot_rows = expert_ids.reshape(-1) * capacity + ranks
    select = (slot_rows[:, None] == jnp.arange(rows_all, dtype=slot_rows.dtype)[None, :]).astype(
        jnp.bfloat16
    )
    per_token = jnp.sum(select.reshape(tok_rows, 2, rows_all), axis=1)
    outgoing = contract(per_token, tokens, 0, 0).astype(jnp.bfloat16)
    arrived = lax.all_to_all(
        outgoing.reshape(experts, capacity, quarter),
        "expert",
        split_axis=0,
        concat_axis=0,
        tiled=True,
    ).reshape(rows_all, quarter)
    both = ring_reduce_scatter(
        jnp.concatenate([contract(arrived, gate_mat, 1, 0), contract(arrived, up_mat, 1, 0)], axis=1)
    )
    gate_pre, up_pre = both[:, :ff], both[:, ff:]
    sigmoid_gate, hidden_part = activate(gate_pre, up_pre)
    hidden = lax.all_gather(hidden_part, "dp", axis=0, tiled=True)
    out_slots = (
        contract(hidden, down_mat, 1, 0).astype(jnp.bfloat16).reshape(experts, capacity, quarter)
    )
    returned = lax.all_to_all(out_slots, "expert", split_axis=0, concat_axis=0, tiled=True).reshape(
        rows_all, quarter
    )
    picked = contract(select, returned, 1, 0).reshape(tok_rows, 2, quarter)
    combined = jnp.sum(gate_weights[:, :, None] * picked, axis=1)
    mixed = combined.astype(jnp.bfloat16)
    row_grad = level_weights[:, None] * (combined - targets.astype(jnp.float32))
    slot_grad = (
        (gate_weights[:, :, None] * row_grad[:, None, :])
        .astype(jnp.bfloat16)
        .reshape(2 * tok_rows, quarter)
    )
    grad_out = contract(select, slot_grad, 0, 0).astype(jnp.bfloat16)
    grad_slots = lax.all_to_all(
        grad_out.reshape(experts, capacity, quarter),
        "expert",
        split_axis=0,
        concat_axis=0,
        tiled=True,
    ).reshape(rows_all, quarter)
    down_grad = contract(hidden, grad_slots, 0, 0)
    hidden_grad = ring_reduce_scatter(contract(grad_slots, down_mat, 1, 1))
    deltas = lax.all_gather(
        jnp.concatenate(derivatives(hidden_grad, gate_pre, up_pre, sigmoid_gate), axis=1),
        "dp",
        axis=0,
        tiled=True,
    )
    gate_delta, up_delta = deltas[:, :ff], deltas[:, ff:]
    input_slots = (contract(gate_delta, gate_mat, 1, 1) + contract(up_delta, up_mat, 1, 1)).astype(
        jnp.bfloat16
    )
    gate_grad = contract(arrived, gate_delta, 0, 0)
    up_grad = contract(arrived, up_delta, 0, 0)
    input_back = lax.all_to_all(
        input_slots.reshape(experts, capacity, quarter),
        "expert",
        split_axis=0,
        concat_axis=0,
        tiled=True,
    ).reshape(rows_all, quarter)
    token_grad = contract(per_token, input_back, 1, 0).astype(jnp.bfloat16)
    return (mixed, token_grad, gate_grad[None], up_grad[None], down_grad[None])


def solution(mesh):
    in_specs = (
        P("expert", "dp"),
        P("expert", "dp"),
        P("expert", None),
        P("expert", None),
        P("expert"),
        P("expert", "dp", None),
        P("expert", "dp", None),
        P("expert", None, "dp"),
    )
    out_specs = (
        P("expert", "dp"),
        P("expert", "dp"),
        P("expert", "dp", None),
        P("expert", "dp", None),
        P("expert", None, "dp"),
    )
    return jax.shard_map(shards, mesh=mesh, in_specs=in_specs, out_specs=out_specs, check_vma=False)
```

```python
import jax
import jax.numpy as jnp
from jax import lax
from jax.sharding import PartitionSpec as P


def slot_ranks(routing, experts):
    listed = routing.reshape(routing.shape[0], -1)
    onehot = (listed[:, :, None] == jnp.arange(experts, dtype=jnp.int32)[None, None, :]).astype(
        jnp.int32
    )
    earlier = jnp.cumsum(onehot, axis=1) - onehot
    return jnp.sum(earlier * onehot, axis=2)


def contract(left, right, left_dim, right_dim):
    return lax.dot_general(
        left, right, (((left_dim,), (right_dim,)), ((), ())), preferred_element_type=jnp.float32
    )


def activate(gate_pre, up_pre):
    sigmoid_gate = jax.nn.sigmoid(gate_pre)
    return (sigmoid_gate, (gate_pre * sigmoid_gate * up_pre).astype(jnp.bfloat16))


def derivatives(hidden_grad, gate_pre, up_pre, sigmoid_gate):
    gate_delta = (
        hidden_grad * up_pre * sigmoid_gate * (1.0 + gate_pre * (1.0 - sigmoid_gate))
    ).astype(jnp.bfloat16)
    up_delta = (hidden_grad * gate_pre * sigmoid_gate).astype(jnp.bfloat16)
    return (gate_delta, up_delta)


def shards(tokens, targets, expert_ids, gate_weights, level_weights, w_gate, w_up, w_down):
    experts = lax.axis_size("expert")
    tok_rows = tokens.shape[0]
    quarter = tokens.shape[1]
    capacity = 4 * tok_rows // experts
    rows_all = experts * capacity
    gate_mat = w_gate[0]
    up_mat = w_up[0]
    down_mat = w_down[0]
    ff = gate_mat.shape[1]
    ranks = slot_ranks(expert_ids.reshape(1, tok_rows, 2), experts).reshape(-1)
    slot_rows = expert_ids.reshape(-1) * capacity + ranks
    select = (slot_rows[:, None] == jnp.arange(rows_all, dtype=slot_rows.dtype)[None, :]).astype(
        jnp.bfloat16
    )
    per_token = jnp.sum(select.reshape(tok_rows, 2, rows_all), axis=1)
    outgoing = contract(per_token, tokens, 0, 0).astype(jnp.bfloat16)
    arrived = lax.all_to_all(
        outgoing.reshape(experts, capacity, quarter),
        "expert",
        split_axis=0,
        concat_axis=0,
        tiled=True,
    ).reshape(rows_all, quarter)
    both = lax.psum_scatter(
        contract(arrived, jnp.concatenate([gate_mat, up_mat], axis=1), 1, 0),
        "dp",
        scatter_dimension=0,
        tiled=True,
    )
    gate_pre, up_pre = both[:, :ff], both[:, ff:]
    sigmoid_gate, hidden_part = activate(gate_pre, up_pre)
    hidden = lax.all_gather(hidden_part, "dp", axis=0, tiled=True)
    out_slots = (
        contract(hidden, down_mat, 1, 0).astype(jnp.bfloat16).reshape(experts, capacity, quarter)
    )
    returned = lax.all_to_all(out_slots, "expert", split_axis=0, concat_axis=0, tiled=True).reshape(
        rows_all, quarter
    )
    pair = select.reshape(tok_rows, 2, rows_all)
    first, second = pair[:, 0], pair[:, 1]
    combined = gate_weights[:, 0:1] * contract(first, returned, 1, 0) + gate_weights[
        :, 1:2
    ] * contract(second, returned, 1, 0)
    mixed = combined.astype(jnp.bfloat16)
    row_grad = level_weights[:, None] * (combined - targets.astype(jnp.float32))
    grad_out = (
        contract(first, (gate_weights[:, 0:1] * row_grad).astype(jnp.bfloat16), 0, 0)
        + contract(second, (gate_weights[:, 1:2] * row_grad).astype(jnp.bfloat16), 0, 0)
    ).astype(jnp.bfloat16)
    grad_slots = lax.all_to_all(
        grad_out.reshape(experts, capacity, quarter),
        "expert",
        split_axis=0,
        concat_axis=0,
        tiled=True,
    ).reshape(rows_all, quarter)
    down_grad = contract(hidden, grad_slots, 0, 0)
    hidden_grad = lax.psum_scatter(
        contract(grad_slots, down_mat, 1, 1), "dp", scatter_dimension=0, tiled=True
    )
    deltas = lax.all_gather(
        jnp.concatenate(derivatives(hidden_grad, gate_pre, up_pre, sigmoid_gate), axis=1),
        "dp",
        axis=0,
        tiled=True,
    )
    gate_delta, up_delta = deltas[:, :ff], deltas[:, ff:]
    input_slots = (contract(gate_delta, gate_mat, 1, 1) + contract(up_delta, up_mat, 1, 1)).astype(
        jnp.bfloat16
    )
    gate_grad = contract(arrived, gate_delta, 0, 0)
    up_grad = contract(arrived, up_delta, 0, 0)
    input_back = lax.all_to_all(
        input_slots.reshape(experts, capacity, quarter),
        "expert",
        split_axis=0,
        concat_axis=0,
        tiled=True,
    ).reshape(rows_all, quarter)
    token_grad = contract(per_token, input_back, 1, 0).astype(jnp.bfloat16)
    return (mixed, token_grad, gate_grad[None], up_grad[None], down_grad[None])


def solution(mesh):
    in_specs = (
        P("expert", "dp"),
        P("expert", "dp"),
        P("expert", None),
        P("expert", None),
        P("expert"),
        P("expert", "dp", None),
        P("expert", "dp", None),
        P("expert", None, "dp"),
    )
    out_specs = (
        P("expert", "dp"),
        P("expert", "dp"),
        P("expert", "dp", None),
        P("expert", "dp", None),
        P("expert", None, "dp"),
    )
    return jax.shard_map(shards, mesh=mesh, in_specs=in_specs, out_specs=out_specs, check_vma=False)
```

```python
import jax
import jax.numpy as jnp
from jax import lax
from jax.sharding import PartitionSpec as P


def slot_ranks(routing, experts):
    listed = routing.reshape(routing.shape[0], -1)
    onehot = (listed[:, :, None] == jnp.arange(experts, dtype=jnp.int32)[None, None, :]).astype(
        jnp.int32
    )
    earlier = jnp.cumsum(onehot, axis=1) - onehot
    return jnp.sum(earlier * onehot, axis=2)


def contract(left, right, left_dim, right_dim):
    return lax.dot_general(
        left, right, (((left_dim,), (right_dim,)), ((), ())), preferred_element_type=jnp.float32
    )


def activate(gate_pre, up_pre):
    sigmoid_gate = jax.nn.sigmoid(gate_pre)
    return (sigmoid_gate, (gate_pre * sigmoid_gate * up_pre).astype(jnp.bfloat16))


def derivatives(hidden_grad, gate_pre, up_pre, sigmoid_gate):
    gate_delta = (
        hidden_grad * up_pre * sigmoid_gate * (1.0 + gate_pre * (1.0 - sigmoid_gate))
    ).astype(jnp.bfloat16)
    up_delta = (hidden_grad * gate_pre * sigmoid_gate).astype(jnp.bfloat16)
    return (gate_delta, up_delta)


def shards(tokens, targets, expert_ids, gate_weights, level_weights, w_gate, w_up, w_down):
    experts = lax.axis_size("expert")
    tok_rows = tokens.shape[0]
    quarter = tokens.shape[1]
    capacity = 4 * tok_rows // experts
    rows_all = experts * capacity
    gate_mat = w_gate[0]
    up_mat = w_up[0]
    down_mat = w_down[0]
    ff = gate_mat.shape[1]
    joined = jnp.concatenate([gate_mat, up_mat], axis=1)
    ranks = slot_ranks(expert_ids.reshape(1, tok_rows, 2), experts).reshape(-1)
    slot_rows = expert_ids.reshape(-1) * capacity + ranks
    select = (slot_rows[:, None] == jnp.arange(rows_all, dtype=slot_rows.dtype)[None, :]).astype(
        jnp.bfloat16
    )
    per_token = jnp.sum(select.reshape(tok_rows, 2, rows_all), axis=1)
    outgoing = contract(per_token, tokens, 0, 0).astype(jnp.bfloat16)
    arrived = lax.all_to_all(
        outgoing.reshape(experts, capacity, quarter),
        "expert",
        split_axis=0,
        concat_axis=0,
        tiled=True,
    ).reshape(rows_all, quarter)
    both = lax.psum_scatter(
        contract(arrived, joined, 1, 0),
        "dp",
        scatter_dimension=0,
        tiled=True,
    )
    gate_pre, up_pre = both[:, :ff], both[:, ff:]
    sigmoid_gate, hidden_part = activate(gate_pre, up_pre)
    hidden = lax.all_gather(hidden_part, "dp", axis=0, tiled=True)
    out_slots = (
        contract(hidden, down_mat, 1, 0).astype(jnp.bfloat16).reshape(experts, capacity, quarter)
    )
    returned = lax.all_to_all(out_slots, "expert", split_axis=0, concat_axis=0, tiled=True).reshape(
        rows_all, quarter
    )
    pair = select.reshape(tok_rows, 2, rows_all)
    first, second = pair[:, 0], pair[:, 1]
    combined = gate_weights[:, 0:1] * contract(first, returned, 1, 0) + gate_weights[
        :, 1:2
    ] * contract(second, returned, 1, 0)
    mixed = combined.astype(jnp.bfloat16)
    row_grad = level_weights[:, None] * (combined - targets.astype(jnp.float32))
    grad_out = (
        contract(first, (gate_weights[:, 0:1] * row_grad).astype(jnp.bfloat16), 0, 0)
        + contract(second, (gate_weights[:, 1:2] * row_grad).astype(jnp.bfloat16), 0, 0)
    ).astype(jnp.bfloat16)
    grad_slots = lax.all_to_all(
        grad_out.reshape(experts, capacity, quarter),
        "expert",
        split_axis=0,
        concat_axis=0,
        tiled=True,
    ).reshape(rows_all, quarter)
    down_grad = contract(hidden, grad_slots, 0, 0)
    hidden_grad = lax.psum_scatter(
        contract(grad_slots, down_mat, 1, 1), "dp", scatter_dimension=0, tiled=True
    )
    deltas = lax.all_gather(
        jnp.concatenate(derivatives(hidden_grad, gate_pre, up_pre, sigmoid_gate), axis=1),
        "dp",
        axis=0,
        tiled=True,
    )
    gate_delta, up_delta = deltas[:, :ff], deltas[:, ff:]
    input_slots = contract(deltas, joined, 1, 1).astype(jnp.bfloat16)
    gate_grad = contract(arrived, gate_delta, 0, 0)
    up_grad = contract(arrived, up_delta, 0, 0)
    input_back = lax.all_to_all(
        input_slots.reshape(experts, capacity, quarter),
        "expert",
        split_axis=0,
        concat_axis=0,
        tiled=True,
    ).reshape(rows_all, quarter)
    token_grad = contract(per_token, input_back, 1, 0).astype(jnp.bfloat16)
    return (mixed, token_grad, gate_grad[None], up_grad[None], down_grad[None])


def solution(mesh):
    in_specs = (
        P("expert", "dp"),
        P("expert", "dp"),
        P("expert", None),
        P("expert", None),
        P("expert"),
        P("expert", "dp", None),
        P("expert", "dp", None),
        P("expert", None, "dp"),
    )
    out_specs = (
        P("expert", "dp"),
        P("expert", "dp"),
        P("expert", "dp", None),
        P("expert", "dp", None),
        P("expert", None, "dp"),
    )
    return jax.shard_map(shards, mesh=mesh, in_specs=in_specs, out_specs=out_specs, check_vma=False)
```

```python
import jax
import jax.numpy as jnp
from jax import lax
from jax.sharding import PartitionSpec as P


def contract(left, right, left_dim, right_dim):
    return lax.dot_general(
        left, right, (((left_dim,), (right_dim,)), ((), ())), preferred_element_type=jnp.float32
    )


def activate(gate_pre, up_pre):
    sigmoid_gate = jax.nn.sigmoid(gate_pre)
    return (sigmoid_gate, (gate_pre * sigmoid_gate * up_pre).astype(jnp.bfloat16))


def derivatives(hidden_grad, gate_pre, up_pre, sigmoid_gate):
    gate_delta = (
        hidden_grad * up_pre * sigmoid_gate * (1.0 + gate_pre * (1.0 - sigmoid_gate))
    ).astype(jnp.bfloat16)
    up_delta = (hidden_grad * gate_pre * sigmoid_gate).astype(jnp.bfloat16)
    return (gate_delta, up_delta)


def shards(tokens, targets, expert_ids, gate_weights, level_weights, w_gate, w_up, w_down):
    experts = lax.axis_size("expert")
    tok_rows = tokens.shape[0]
    quarter = tokens.shape[1]
    capacity = 4 * tok_rows // experts
    rows_all = experts * capacity
    gate_mat = w_gate[0]
    up_mat = w_up[0]
    down_mat = w_down[0]
    ff = gate_mat.shape[1]
    listed = expert_ids.reshape(-1)
    order = jnp.arange(2 * tok_rows, dtype=jnp.int32)
    onehot = (listed[:, None] == jnp.arange(experts, dtype=jnp.int32)[None, :]).astype(jnp.bfloat16)
    before = (order[None, :] < order[:, None]).astype(jnp.bfloat16)
    counts = contract(before, onehot, 1, 0)
    ranks = jnp.sum(counts * onehot.astype(jnp.float32), axis=1).astype(jnp.int32)
    slot_rows = (listed * capacity + ranks).reshape(tok_rows, 2).T.reshape(-1)
    select = (slot_rows[:, None] == jnp.arange(rows_all, dtype=slot_rows.dtype)[None, :]).astype(
        jnp.bfloat16
    )
    per_token = select[:tok_rows] + select[tok_rows:]
    outgoing = contract(per_token, tokens, 0, 0).astype(jnp.bfloat16)
    arrived = lax.all_to_all(
        outgoing.reshape(experts, capacity, quarter),
        "expert",
        split_axis=0,
        concat_axis=0,
        tiled=True,
    ).reshape(rows_all, quarter)
    both = lax.psum_scatter(
        contract(arrived, jnp.concatenate([gate_mat, up_mat], axis=1), 1, 0),
        "dp",
        scatter_dimension=0,
        tiled=True,
    )
    gate_pre, up_pre = both[:, :ff], both[:, ff:]
    sigmoid_gate, hidden_part = activate(gate_pre, up_pre)
    hidden = lax.all_gather(hidden_part, "dp", axis=0, tiled=True)
    out_slots = (
        contract(hidden, down_mat, 1, 0).astype(jnp.bfloat16).reshape(experts, capacity, quarter)
    )
    returned = lax.all_to_all(out_slots, "expert", split_axis=0, concat_axis=0, tiled=True).reshape(
        rows_all, quarter
    )
    picked = contract(select, returned, 1, 0)
    combined = (
        gate_weights[:, 0:1] * picked[:tok_rows] + gate_weights[:, 1:2] * picked[tok_rows:]
    )
    mixed = combined.astype(jnp.bfloat16)
    row_grad = level_weights[:, None] * (combined - targets.astype(jnp.float32))
    slot_grad = jnp.concatenate(
        [gate_weights[:, 0:1] * row_grad, gate_weights[:, 1:2] * row_grad], axis=0
    ).astype(jnp.bfloat16)
    grad_out = contract(select, slot_grad, 0, 0).astype(jnp.bfloat16)
    grad_slots = lax.all_to_all(
        grad_out.reshape(experts, capacity, quarter),
        "expert",
        split_axis=0,
        concat_axis=0,
        tiled=True,
    ).reshape(rows_all, quarter)
    down_grad = contract(hidden, grad_slots, 0, 0)
    hidden_grad = lax.psum_scatter(
        contract(grad_slots, down_mat, 1, 1), "dp", scatter_dimension=0, tiled=True
    )
    deltas = lax.all_gather(
        jnp.concatenate(derivatives(hidden_grad, gate_pre, up_pre, sigmoid_gate), axis=1),
        "dp",
        axis=0,
        tiled=True,
    )
    gate_delta, up_delta = deltas[:, :ff], deltas[:, ff:]
    input_slots = (contract(gate_delta, gate_mat, 1, 1) + contract(up_delta, up_mat, 1, 1)).astype(
        jnp.bfloat16
    )
    gate_grad = contract(arrived, gate_delta, 0, 0)
    up_grad = contract(arrived, up_delta, 0, 0)
    input_back = lax.all_to_all(
        input_slots.reshape(experts, capacity, quarter),
        "expert",
        split_axis=0,
        concat_axis=0,
        tiled=True,
    ).reshape(rows_all, quarter)
    token_grad = contract(per_token, input_back, 1, 0).astype(jnp.bfloat16)
    return (mixed, token_grad, gate_grad[None], up_grad[None], down_grad[None])


def solution(mesh):
    in_specs = (
        P("expert", "dp"),
        P("expert", "dp"),
        P("expert", None),
        P("expert", None),
        P("expert"),
        P("expert", "dp", None),
        P("expert", "dp", None),
        P("expert", None, "dp"),
    )
    out_specs = (
        P("expert", "dp"),
        P("expert", "dp"),
        P("expert", "dp", None),
        P("expert", "dp", None),
        P("expert", None, "dp"),
    )
    return jax.shard_map(shards, mesh=mesh, in_specs=in_specs, out_specs=out_specs, check_vma=False)
```

```python
import jax
import jax.numpy as jnp
from jax import lax
from jax.sharding import PartitionSpec as P


def contract(left, right, left_dim, right_dim):
    return lax.dot_general(
        left, right, (((left_dim,), (right_dim,)), ((), ())), preferred_element_type=jnp.float32
    )


def activate(gate_pre, up_pre):
    sigmoid_gate = jax.nn.sigmoid(gate_pre)
    return (sigmoid_gate, (gate_pre * sigmoid_gate * up_pre).astype(jnp.bfloat16))


def derivatives(hidden_grad, gate_pre, up_pre, sigmoid_gate):
    gate_delta = (
        hidden_grad * up_pre * sigmoid_gate * (1.0 + gate_pre * (1.0 - sigmoid_gate))
    ).astype(jnp.bfloat16)
    up_delta = (hidden_grad * gate_pre * sigmoid_gate).astype(jnp.bfloat16)
    return (gate_delta, up_delta)


def shards(tokens, targets, expert_ids, gate_weights, level_weights, w_gate, w_up, w_down):
    experts = lax.axis_size("expert")
    tok_rows = tokens.shape[0]
    quarter = tokens.shape[1]
    capacity = 4 * tok_rows // experts
    rows_all = experts * capacity
    gate_mat = w_gate[0]
    up_mat = w_up[0]
    down_mat = w_down[0]
    ff = gate_mat.shape[1]
    listed = expert_ids.reshape(-1)
    order = jnp.arange(2 * tok_rows, dtype=jnp.int32)
    onehot = (listed[:, None] == jnp.arange(experts, dtype=jnp.int32)[None, :]).astype(jnp.bfloat16)
    before = (order[None, :] < order[:, None]).astype(jnp.bfloat16)
    counts = contract(before, onehot, 1, 0)
    ranks = jnp.sum(counts * onehot.astype(jnp.float32), axis=1).astype(jnp.int32)
    slot_rows = (listed * capacity + ranks).reshape(tok_rows, 2).T.reshape(-1)
    select = (slot_rows[:, None] == jnp.arange(rows_all, dtype=slot_rows.dtype)[None, :]).astype(
        jnp.bfloat16
    )
    per_token = select[:tok_rows] + select[tok_rows:]
    outgoing = contract(per_token, tokens, 0, 0).astype(jnp.bfloat16)
    arrived = lax.all_to_all(
        outgoing.reshape(experts, capacity, quarter),
        "expert",
        split_axis=0,
        concat_axis=0,
        tiled=True,
    ).reshape(rows_all, quarter)
    both = lax.psum_scatter(
        contract(arrived, jnp.concatenate([gate_mat, up_mat], axis=1), 1, 0),
        "dp",
        scatter_dimension=0,
        tiled=True,
    )
    gate_pre, up_pre = both[:, :ff], both[:, ff:]
    sigmoid_gate, hidden_part = activate(gate_pre, up_pre)
    hidden = lax.all_gather(hidden_part, "dp", axis=0, tiled=True)
    out_slots = (
        contract(hidden, down_mat, 1, 0).astype(jnp.bfloat16).reshape(experts, capacity, quarter)
    )
    returned = lax.all_to_all(out_slots, "expert", split_axis=0, concat_axis=0, tiled=True).reshape(
        rows_all, quarter
    )
    picked = contract(select, returned, 1, 0)
    combined = (
        gate_weights[:, 0:1] * picked[:tok_rows] + gate_weights[:, 1:2] * picked[tok_rows:]
    )
    mixed = combined.astype(jnp.bfloat16)
    row_grad = level_weights[:, None] * (combined - targets.astype(jnp.float32))
    slot_grad = jnp.concatenate(
        [gate_weights[:, 0:1] * row_grad, gate_weights[:, 1:2] * row_grad], axis=0
    ).astype(jnp.bfloat16)
    grad_out = contract(select, slot_grad, 0, 0).astype(jnp.bfloat16)
    grad_slots = lax.all_to_all(
        grad_out.reshape(experts, capacity, quarter),
        "expert",
        split_axis=0,
        concat_axis=0,
        tiled=True,
    ).reshape(rows_all, quarter)
    down_grad = contract(hidden, grad_slots, 0, 0)
    hidden_grad = lax.psum_scatter(
        contract(grad_slots, down_mat, 1, 1), "dp", scatter_dimension=0, tiled=True
    )
    hidden_grad, down_grad = lax.optimization_barrier((hidden_grad, down_grad))
    deltas = lax.all_gather(
        jnp.concatenate(derivatives(hidden_grad, gate_pre, up_pre, sigmoid_gate), axis=1),
        "dp",
        axis=0,
        tiled=True,
    )
    gate_delta, up_delta = deltas[:, :ff], deltas[:, ff:]
    input_slots = (contract(gate_delta, gate_mat, 1, 1) + contract(up_delta, up_mat, 1, 1)).astype(
        jnp.bfloat16
    )
    gate_grad = contract(arrived, gate_delta, 0, 0)
    up_grad = contract(arrived, up_delta, 0, 0)
    input_back = lax.all_to_all(
        input_slots.reshape(experts, capacity, quarter),
        "expert",
        split_axis=0,
        concat_axis=0,
        tiled=True,
    ).reshape(rows_all, quarter)
    token_grad = contract(per_token, input_back, 1, 0).astype(jnp.bfloat16)
    return (mixed, token_grad, gate_grad[None], up_grad[None], down_grad[None])


def solution(mesh):
    in_specs = (
        P("expert", "dp"),
        P("expert", "dp"),
        P("expert", None),
        P("expert", None),
        P("expert"),
        P("expert", "dp", None),
        P("expert", "dp", None),
        P("expert", None, "dp"),
    )
    out_specs = (
        P("expert", "dp"),
        P("expert", "dp"),
        P("expert", "dp", None),
        P("expert", "dp", None),
        P("expert", None, "dp"),
    )
    return jax.shard_map(shards, mesh=mesh, in_specs=in_specs, out_specs=out_specs, check_vma=False)
```

```python
import jax
import jax.numpy as jnp
from jax import lax
from jax.sharding import PartitionSpec as P


def contract(left, right, left_dim, right_dim):
    return lax.dot_general(
        left, right, (((left_dim,), (right_dim,)), ((), ())), preferred_element_type=jnp.float32
    )


def activate(gate_pre, up_pre):
    sigmoid_gate = jax.nn.sigmoid(gate_pre)
    return (sigmoid_gate, (gate_pre * sigmoid_gate * up_pre).astype(jnp.bfloat16))


def shards(tokens, targets, expert_ids, gate_weights, level_weights, w_gate, w_up, w_down):
    experts = lax.axis_size("expert")
    tok_rows = tokens.shape[0]
    quarter = tokens.shape[1]
    capacity = 4 * tok_rows // experts
    rows_all = experts * capacity
    gate_mat = w_gate[0]
    up_mat = w_up[0]
    down_mat = w_down[0]
    ff = gate_mat.shape[1]
    listed = expert_ids.reshape(-1)
    order = jnp.arange(2 * tok_rows, dtype=jnp.int32)
    onehot = (listed[:, None] == jnp.arange(experts, dtype=jnp.int32)[None, :]).astype(jnp.bfloat16)
    before = (order[None, :] < order[:, None]).astype(jnp.bfloat16)
    counts = contract(before, onehot, 1, 0)
    ranks = jnp.sum(counts * onehot.astype(jnp.float32), axis=1).astype(jnp.int32)
    slot_rows = (listed * capacity + ranks).reshape(tok_rows, 2).T.reshape(-1)
    select = (slot_rows[:, None] == jnp.arange(rows_all, dtype=slot_rows.dtype)[None, :]).astype(
        jnp.bfloat16
    )
    per_token = select[:tok_rows] + select[tok_rows:]
    outgoing = contract(per_token, tokens, 0, 0).astype(jnp.bfloat16)
    arrived = lax.all_to_all(
        outgoing.reshape(experts, capacity, quarter),
        "expert",
        split_axis=0,
        concat_axis=0,
        tiled=True,
    ).reshape(rows_all, quarter)
    both = lax.psum_scatter(
        contract(arrived, jnp.concatenate([gate_mat, up_mat], axis=1), 1, 0),
        "dp",
        scatter_dimension=0,
        tiled=True,
    )
    gate_pre, up_pre = both[:, :ff], both[:, ff:]
    sigmoid_gate, hidden_part = activate(gate_pre, up_pre)
    hidden = lax.all_gather(hidden_part, "dp", axis=0, tiled=True)
    out_slots = (
        contract(hidden, down_mat, 1, 0).astype(jnp.bfloat16).reshape(experts, capacity, quarter)
    )
    returned = lax.all_to_all(out_slots, "expert", split_axis=0, concat_axis=0, tiled=True).reshape(
        rows_all, quarter
    )
    picked = contract(select, returned, 1, 0)
    combined = (
        gate_weights[:, 0:1] * picked[:tok_rows] + gate_weights[:, 1:2] * picked[tok_rows:]
    )
    mixed = combined.astype(jnp.bfloat16)
    row_grad = level_weights[:, None] * (combined - targets.astype(jnp.float32))
    slot_grad = jnp.concatenate(
        [gate_weights[:, 0:1] * row_grad, gate_weights[:, 1:2] * row_grad], axis=0
    ).astype(jnp.bfloat16)
    grad_out = contract(select, slot_grad, 0, 0).astype(jnp.bfloat16)
    grad_slots = lax.all_to_all(
        grad_out.reshape(experts, capacity, quarter),
        "expert",
        split_axis=0,
        concat_axis=0,
        tiled=True,
    ).reshape(rows_all, quarter)
    down_grad = contract(hidden, grad_slots, 0, 0)
    hidden_grad = lax.psum_scatter(
        contract(grad_slots, down_mat, 1, 1), "dp", scatter_dimension=0, tiled=True
    )
    twice = jnp.concatenate([hidden_grad, hidden_grad], axis=1)
    deltas = lax.all_gather(
        (
            twice
            * jnp.concatenate([up_pre, gate_pre], axis=1)
            * jnp.concatenate([sigmoid_gate, sigmoid_gate], axis=1)
            * jnp.concatenate(
                [1.0 + gate_pre * (1.0 - sigmoid_gate), jnp.ones_like(gate_pre)], axis=1
            )
        ).astype(jnp.bfloat16),
        "dp",
        axis=0,
        tiled=True,
    )
    gate_delta, up_delta = deltas[:, :ff], deltas[:, ff:]
    input_slots = (contract(gate_delta, gate_mat, 1, 1) + contract(up_delta, up_mat, 1, 1)).astype(
        jnp.bfloat16
    )
    gate_grad = contract(arrived, gate_delta, 0, 0)
    up_grad = contract(arrived, up_delta, 0, 0)
    input_back = lax.all_to_all(
        input_slots.reshape(experts, capacity, quarter),
        "expert",
        split_axis=0,
        concat_axis=0,
        tiled=True,
    ).reshape(rows_all, quarter)
    token_grad = contract(per_token, input_back, 1, 0).astype(jnp.bfloat16)
    return (mixed, token_grad, gate_grad[None], up_grad[None], down_grad[None])


def solution(mesh):
    in_specs = (
        P("expert", "dp"),
        P("expert", "dp"),
        P("expert", None),
        P("expert", None),
        P("expert"),
        P("expert", "dp", None),
        P("expert", "dp", None),
        P("expert", None, "dp"),
    )
    out_specs = (
        P("expert", "dp"),
        P("expert", "dp"),
        P("expert", "dp", None),
        P("expert", "dp", None),
        P("expert", None, "dp"),
    )
    return jax.shard_map(shards, mesh=mesh, in_specs=in_specs, out_specs=out_specs, check_vma=False)
```

```python
import jax
import jax.numpy as jnp
from jax import lax
from jax.sharding import PartitionSpec as P


def contract(left, right, left_dim, right_dim):
    return lax.dot_general(
        left, right, (((left_dim,), (right_dim,)), ((), ())), preferred_element_type=jnp.float32
    )


def activate(gate_pre, up_pre):
    sigmoid_gate = jax.nn.sigmoid(gate_pre)
    return (sigmoid_gate, (gate_pre * sigmoid_gate * up_pre).astype(jnp.bfloat16))


def derivatives(hidden_grad, gate_pre, up_pre, sigmoid_gate):
    gate_delta = (
        hidden_grad * up_pre * sigmoid_gate * (1.0 + gate_pre * (1.0 - sigmoid_gate))
    ).astype(jnp.bfloat16)
    up_delta = (hidden_grad * gate_pre * sigmoid_gate).astype(jnp.bfloat16)
    return (gate_delta, up_delta)


def shards(tokens, targets, expert_ids, gate_weights, level_weights, w_gate, w_up, w_down):
    experts = lax.axis_size("expert")
    tok_rows = tokens.shape[0]
    quarter = tokens.shape[1]
    capacity = 4 * tok_rows // experts
    rows_all = experts * capacity
    gate_mat = w_gate[0]
    up_mat = w_up[0]
    down_mat = w_down[0]
    ff = gate_mat.shape[1]
    listed = expert_ids.reshape(-1)
    order = jnp.arange(2 * tok_rows, dtype=jnp.int32)
    onehot = (listed[:, None] == jnp.arange(experts, dtype=jnp.int32)[None, :]).astype(jnp.bfloat16)
    before = (order[None, :] < order[:, None]).astype(jnp.bfloat16)
    counts = contract(before, onehot, 1, 0)
    ranks = jnp.sum(counts * onehot.astype(jnp.float32), axis=1).astype(jnp.int32)
    slot_rows = (listed * capacity + ranks).reshape(tok_rows, 2).T.reshape(-1)
    select = (slot_rows[:, None] == jnp.arange(rows_all, dtype=slot_rows.dtype)[None, :]).astype(
        jnp.bfloat16
    )
    per_token = select[:tok_rows] + select[tok_rows:]
    select, per_token = lax.optimization_barrier((select, per_token))
    outgoing = contract(per_token, tokens, 0, 0).astype(jnp.bfloat16)
    arrived = lax.all_to_all(
        outgoing.reshape(experts, capacity, quarter),
        "expert",
        split_axis=0,
        concat_axis=0,
        tiled=True,
    ).reshape(rows_all, quarter)
    both = lax.psum_scatter(
        contract(arrived, jnp.concatenate([gate_mat, up_mat], axis=1), 1, 0),
        "dp",
        scatter_dimension=0,
        tiled=True,
    )
    gate_pre, up_pre = both[:, :ff], both[:, ff:]
    sigmoid_gate, hidden_part = activate(gate_pre, up_pre)
    hidden = lax.all_gather(hidden_part, "dp", axis=0, tiled=True)
    out_slots = (
        contract(hidden, down_mat, 1, 0).astype(jnp.bfloat16).reshape(experts, capacity, quarter)
    )
    returned = lax.all_to_all(out_slots, "expert", split_axis=0, concat_axis=0, tiled=True).reshape(
        rows_all, quarter
    )
    picked = contract(select, returned, 1, 0)
    combined = (
        gate_weights[:, 0:1] * picked[:tok_rows] + gate_weights[:, 1:2] * picked[tok_rows:]
    )
    mixed = combined.astype(jnp.bfloat16)
    row_grad = level_weights[:, None] * (combined - targets.astype(jnp.float32))
    slot_grad = jnp.concatenate(
        [gate_weights[:, 0:1] * row_grad, gate_weights[:, 1:2] * row_grad], axis=0
    ).astype(jnp.bfloat16)
    grad_out = contract(select, slot_grad, 0, 0).astype(jnp.bfloat16)
    grad_slots = lax.all_to_all(
        grad_out.reshape(experts, capacity, quarter),
        "expert",
        split_axis=0,
        concat_axis=0,
        tiled=True,
    ).reshape(rows_all, quarter)
    down_grad = contract(hidden, grad_slots, 0, 0)
    hidden_grad = lax.psum_scatter(
        contract(grad_slots, down_mat, 1, 1), "dp", scatter_dimension=0, tiled=True
    )
    deltas = lax.all_gather(
        jnp.concatenate(derivatives(hidden_grad, gate_pre, up_pre, sigmoid_gate), axis=1),
        "dp",
        axis=0,
        tiled=True,
    )
    gate_delta, up_delta = deltas[:, :ff], deltas[:, ff:]
    input_slots = (contract(gate_delta, gate_mat, 1, 1) + contract(up_delta, up_mat, 1, 1)).astype(
        jnp.bfloat16
    )
    gate_grad = contract(arrived, gate_delta, 0, 0)
    up_grad = contract(arrived, up_delta, 0, 0)
    input_back = lax.all_to_all(
        input_slots.reshape(experts, capacity, quarter),
        "expert",
        split_axis=0,
        concat_axis=0,
        tiled=True,
    ).reshape(rows_all, quarter)
    token_grad = contract(per_token, input_back, 1, 0).astype(jnp.bfloat16)
    return (mixed, token_grad, gate_grad[None], up_grad[None], down_grad[None])


def solution(mesh):
    in_specs = (
        P("expert", "dp"),
        P("expert", "dp"),
        P("expert", None),
        P("expert", None),
        P("expert"),
        P("expert", "dp", None),
        P("expert", "dp", None),
        P("expert", None, "dp"),
    )
    out_specs = (
        P("expert", "dp"),
        P("expert", "dp"),
        P("expert", "dp", None),
        P("expert", "dp", None),
        P("expert", None, "dp"),
    )
    return jax.shard_map(shards, mesh=mesh, in_specs=in_specs, out_specs=out_specs, check_vma=False)
```

```python
import jax
import jax.numpy as jnp
from jax import lax
from jax.sharding import PartitionSpec as P


def contract(left, right, left_dim, right_dim):
    return lax.dot_general(
        left, right, (((left_dim,), (right_dim,)), ((), ())), preferred_element_type=jnp.float32
    )


def activate(gate_pre, up_pre):
    sigmoid_gate = jax.nn.sigmoid(gate_pre)
    return (sigmoid_gate, (gate_pre * sigmoid_gate * up_pre).astype(jnp.bfloat16))


def derivatives(hidden_grad, gate_pre, up_pre, sigmoid_gate):
    gate_delta = (
        hidden_grad * up_pre * sigmoid_gate * (1.0 + gate_pre * (1.0 - sigmoid_gate))
    ).astype(jnp.bfloat16)
    up_delta = (hidden_grad * gate_pre * sigmoid_gate).astype(jnp.bfloat16)
    return (gate_delta, up_delta)


def shards(tokens, targets, expert_ids, gate_weights, level_weights, w_gate, w_up, w_down):
    experts = lax.axis_size("expert")
    tok_rows = tokens.shape[0]
    quarter = tokens.shape[1]
    capacity = 4 * tok_rows // experts
    rows_all = experts * capacity
    gate_mat = w_gate[0]
    up_mat = w_up[0]
    down_mat = w_down[0]
    ff = gate_mat.shape[1]
    listed = expert_ids.T.reshape(-1)
    place = jnp.arange(2 * tok_rows, dtype=jnp.int32)
    order = 2 * (place % tok_rows) + place // tok_rows
    onehot = (listed[:, None] == jnp.arange(experts, dtype=jnp.int32)[None, :]).astype(jnp.bfloat16)
    before = (order[None, :] < order[:, None]).astype(jnp.bfloat16)
    counts = contract(before, onehot, 1, 0)
    ranks = jnp.sum(counts * onehot.astype(jnp.float32), axis=1).astype(jnp.int32)
    slot_rows = listed * capacity + ranks
    select = (slot_rows[:, None] == jnp.arange(rows_all, dtype=slot_rows.dtype)[None, :]).astype(
        jnp.bfloat16
    )
    per_token = select[:tok_rows] + select[tok_rows:]
    select, per_token = lax.optimization_barrier((select, per_token))
    outgoing = contract(per_token, tokens, 0, 0).astype(jnp.bfloat16)
    arrived = lax.all_to_all(
        outgoing.reshape(experts, capacity, quarter),
        "expert",
        split_axis=0,
        concat_axis=0,
        tiled=True,
    ).reshape(rows_all, quarter)
    both = lax.psum_scatter(
        contract(arrived, jnp.concatenate([gate_mat, up_mat], axis=1), 1, 0),
        "dp",
        scatter_dimension=0,
        tiled=True,
    )
    gate_pre, up_pre = both[:, :ff], both[:, ff:]
    sigmoid_gate, hidden_part = activate(gate_pre, up_pre)
    hidden = lax.all_gather(hidden_part, "dp", axis=0, tiled=True)
    out_slots = (
        contract(hidden, down_mat, 1, 0).astype(jnp.bfloat16).reshape(experts, capacity, quarter)
    )
    returned = lax.all_to_all(out_slots, "expert", split_axis=0, concat_axis=0, tiled=True).reshape(
        rows_all, quarter
    )
    picked = contract(select, returned, 1, 0)
    combined = (
        gate_weights[:, 0:1] * picked[:tok_rows] + gate_weights[:, 1:2] * picked[tok_rows:]
    )
    mixed = combined.astype(jnp.bfloat16)
    row_grad = level_weights[:, None] * (combined - targets.astype(jnp.float32))
    slot_grad = jnp.concatenate(
        [gate_weights[:, 0:1] * row_grad, gate_weights[:, 1:2] * row_grad], axis=0
    ).astype(jnp.bfloat16)
    grad_out = contract(select, slot_grad, 0, 0).astype(jnp.bfloat16)
    grad_slots = lax.all_to_all(
        grad_out.reshape(experts, capacity, quarter),
        "expert",
        split_axis=0,
        concat_axis=0,
        tiled=True,
    ).reshape(rows_all, quarter)
    down_grad = contract(hidden, grad_slots, 0, 0)
    hidden_grad = lax.psum_scatter(
        contract(grad_slots, down_mat, 1, 1), "dp", scatter_dimension=0, tiled=True
    )
    deltas = lax.all_gather(
        jnp.concatenate(derivatives(hidden_grad, gate_pre, up_pre, sigmoid_gate), axis=1),
        "dp",
        axis=0,
        tiled=True,
    )
    gate_delta, up_delta = deltas[:, :ff], deltas[:, ff:]
    input_slots = (contract(gate_delta, gate_mat, 1, 1) + contract(up_delta, up_mat, 1, 1)).astype(
        jnp.bfloat16
    )
    gate_grad = contract(arrived, gate_delta, 0, 0)
    up_grad = contract(arrived, up_delta, 0, 0)
    input_back = lax.all_to_all(
        input_slots.reshape(experts, capacity, quarter),
        "expert",
        split_axis=0,
        concat_axis=0,
        tiled=True,
    ).reshape(rows_all, quarter)
    token_grad = contract(per_token, input_back, 1, 0).astype(jnp.bfloat16)
    return (mixed, token_grad, gate_grad[None], up_grad[None], down_grad[None])


def solution(mesh):
    in_specs = (
        P("expert", "dp"),
        P("expert", "dp"),
        P("expert", None),
        P("expert", None),
        P("expert"),
        P("expert", "dp", None),
        P("expert", "dp", None),
        P("expert", None, "dp"),
    )
    out_specs = (
        P("expert", "dp"),
        P("expert", "dp"),
        P("expert", "dp", None),
        P("expert", "dp", None),
        P("expert", None, "dp"),
    )
    return jax.shard_map(shards, mesh=mesh, in_specs=in_specs, out_specs=out_specs, check_vma=False)
```
